768 devices in a mesh: seq: 96 (over z, y), head: 8 (over x, core).
Axes of the slice: x: 4, y: 8, z: 12, core: 2. Of those that a mesh axis runs over, the one named last changes fastest.
Arguments:
- query_vectors: bfloat16 [46080, 6144], P('seq', 'head'), may hold values from -250 to 250
- key_vectors: bfloat16 [46080, 6144], P('seq', 'head'), may hold values from -6 to 6
- value_vectors: bfloat16 [46080, 6144], P('seq', 'head'), may hold values from -2.5 to 2.5
- doc_ids: int32 [46080], P('seq'), may hold values from 0 to 191, never falling along the last dimension, each value on 1 to 960 neighbouring positions
- gradients: bfloat16 [192, 128, 7168], P('seq', 'head'), may hold values from -600 to 600
- weights: bfloat16 [192, 128, 7168], P('seq', None, 'head'), may hold values from -2.5 to 2.5
Outputs:
- attention_out: bfloat16 [46080, 6144], P('seq', 'head')
- update: bfloat16 [192, 128, 7168], P('seq', None, 'head')
- new_weights: bfloat16 [192, 128, 7168], P('seq', None, 'head')
The draws below stay inside these ranges and needn't reach their ends.
Inputs may be any that keep to these rules, and one draw needn't show every extreme that they name: `doc_ids`: document ids never fall along the sequence; every document has 1 to 960 tokens and one has exactly 960.
All inputs are finite; a program needn't handle non-finite values.
Results may differ from the reference program's by a relative error of at most 0.0034.
Values may be sent and summed in bfloat16 or wider, within the bound.
No kernel may reach another device: no remote copies, remote signals or barrier semaphores. Data moves between devices by JAX's collectives and lax.ppermute only.
A program may use at most 32 MiB of HBM per device.

```python
import math
import jax
import jax.numpy as jnp
import numpy as np
from jax import lax

D = 7168
HD = 128
TOK_DEV = 480
REACH = 2
NS_ITERS = 5
HEADS = 48
TOKENS = 46080
DOC_MOST = 960
DOCS = 192
MATS = 192


def planted_pair(key):
    blocks = TOKENS // TOK_DEV
    seed_list = jax.random.split(jax.random.fold_in(key, 11), 5)
    full_shape = (TOKENS, HEADS, HD)
    key_base = jnp.clip(jax.random.normal(seed_list[0], full_shape, jnp.float32), -6.0, 6.0)
    query_base = jnp.clip(jax.random.normal(seed_list[1], full_shape, jnp.float32), -6.0, 6.0)
    low_end, high_end, head_low, head_high = (20.0, 150.0, 0.25, 2.5)
    offsets = jax.random.randint(seed_list[2], (blocks, 1, HEADS), 1, TOK_DEV)
    planted_grid = jnp.arange(TOK_DEV, dtype=jnp.int32)[None, :, None] == offsets
    strength = jnp.exp(jax.random.uniform(seed_list[3], (blocks, 1, HEADS), jnp.float32, math.log(low_end), math.log(high_end)))
    strength = strength * jnp.exp(jax.random.uniform(seed_list[4], (1, 1, HEADS), jnp.float32, math.log(head_low), math.log(head_high)))
    strength = jnp.broadcast_to(strength, (blocks, TOK_DEV, HEADS)).reshape(TOKENS, HEADS)
    planted = planted_grid.reshape(TOKENS, HEADS)
    before = jnp.roll(planted, -1, axis=0)
    next_strength = jnp.roll(strength, -1, axis=0)
    next_key = jnp.roll(key_base, -1, axis=0)
    key_final = jnp.where(before[:, :, None], next_key * (1.0 - 2.0 / next_strength)[:, :, None], key_base)
    query_final = jnp.where(planted[:, :, None], key_base * (strength / math.sqrt(HD))[:, :, None], query_base)
    return (query_final.reshape(TOKENS, HEADS * HD), key_final.reshape(TOKENS, HEADS * HD))


def draw_query_vectors(key, part):
    return planted_pair(key)[0].astype(jnp.bfloat16)


def draw_key_vectors(key, part):
    return planted_pair(key)[1].astype(jnp.bfloat16)


def draw_gradients(key, part):
    seed_list = jax.random.split(jax.random.fold_in(key, 23), 3)
    full_shape = (MATS, HD, D)
    row_scale = jnp.exp(jax.random.uniform(seed_list[0], (MATS, 1, D), jnp.float32, 0.0, math.log(10.0)))
    col_scale = jnp.exp(jax.random.uniform(seed_list[1], (MATS, HD, 1), jnp.float32, 0.0, math.log(10.0)))
    row_ramp = jnp.arange(D, dtype=jnp.float32)[None, None, :] / D
    noise_part = jnp.clip(jax.random.normal(seed_list[2], full_shape, jnp.float32), -6.0, 6.0)
    entries = noise_part * jnp.exp(math.log(3.0) * row_ramp)
    return (0.1 * entries * row_scale * col_scale).astype(jnp.bfloat16)


def block_levels(key, shape, cuts, smallest, top_value):
    def one(position, parts):
        steps = jax.random.uniform(jax.random.fold_in(jax.random.fold_in(key, 6), position), (parts,), jnp.float32, smallest / len(cuts), top_value / len(cuts))
        return jnp.repeat(jnp.exp(steps), shape[position] // parts).reshape((-1,) + (1,) * (len(shape) - position - 1))

    level = one(*cuts[0])
    for cut in cuts[1:]:
        level = level * one(*cut)
    return level


def length_profile(number_of, total, bound, lean):
    loads = [(1 << 20) // math.isqrt(standing ** lean) + 1 for standing in range(2, number_of + 1)]
    rest, counts = total - bound - (number_of - 1), [1] * (number_of - 1)
    while rest > 0:
        movable = [i for i in range(number_of - 1) if counts[i] < bound]
        whole, budget = sum([loads[i] for i in movable]), rest
        for i in movable:
            addition = min(bound - counts[i], max(1, budget * loads[i] // whole), rest)
            counts[i] = counts[i] + addition
            rest = rest - addition
    return np.array([bound] + counts)


def uneven(stream_key, count, total, bound, lean):
    if count == 2:
        one = jax.random.randint(stream_key, (), max(1, total - bound), min(bound, total - 1) + 1)
        return jnp.stack([one, total - one])
    lengths = jnp.asarray(length_profile(count, total, bound, lean), jnp.int32)
    pairs = (count - 1) // 2
    source_of, sink = lengths[1:1 + 2 * pairs:2], lengths[2:2 + 2 * pairs:2]
    slack = jnp.minimum(source_of - 1, bound - sink)
    passed = jax.random.randint(jax.random.fold_in(stream_key, 1), (pairs,), 0, 1 << 20) % (slack + 1)
    lengths = lengths.at[1:1 + 2 * pairs:2].set(source_of - passed).at[2:2 + 2 * pairs:2].set(sink + passed)
    return lengths[jax.random.permutation(jax.random.fold_in(stream_key, 2), count)]


def bell_draw(rng, dims, deviation, limit, pieces=(), held_as=jnp.bfloat16):
    values = jax.random.normal(rng, dims, jnp.float32) * deviation
    if len(pieces) > 0:
        values = block_levels(rng, dims, pieces, -0.22, 0.18) * values
    return jnp.clip(values, min=-limit, max=limit).astype(held_as)


def setup_inputs(seed: int = 0) -> dict:
    key_of = jax.random.split(jax.random.key(seed), 7)
    query_vectors = draw_query_vectors(jax.random.fold_in(key_of[6], 71), 0)
    key_vectors = draw_key_vectors(jax.random.fold_in(key_of[6], 71), 0)
    value_vectors = bell_draw(key_of[2], (TOKENS, HEADS * HD), 0.4, 2.5, ((0, 96), (1, 8)))
    doc_ids = jnp.searchsorted(jnp.cumsum(uneven(key_of[3], DOCS, TOKENS, DOC_MOST, 2)), jnp.arange(TOKENS), side="right").astype(jnp.int32)
    gradients = draw_gradients(jax.random.fold_in(key_of[6], 71), 0)
    weights = bell_draw(key_of[5], (MATS, HD, D), 0.3, 2.5, ((0, 96), (2, 8)))
    return {"query_vectors": query_vectors, "key_vectors": key_vectors, "value_vectors": value_vectors, "doc_ids": doc_ids, "gradients": gradients, "weights": weights}


first_coef = 3.4445
second_coef = -4.775
third_coef = 2.0315
clip_tau = 100.0
learn_rate = 0.1
decay_rate = 0.1
norm_eps = 1e-07
update_gain = 0.2
masked_fill = -1e+30

def block_attention(query_block, key_window, value_window, same_doc):
    scores = jnp.einsum('qhd,khd->hqk', query_block.astype(jnp.float32), key_window.astype(jnp.float32)) / math.sqrt(HD)
    masked = jnp.where(same_doc[None, :, :], scores, masked_fill)
    row_max = lax.optimization_barrier(jnp.max(masked, axis=2))
    exp_scores = jnp.exp(masked - row_max[:, :, None])
    row_total = lax.optimization_barrier(jnp.sum(exp_scores, axis=2))
    rounded = lax.optimization_barrier(exp_scores.astype(jnp.bfloat16))
    mixed_rows = jnp.einsum('hqk,khd->qhd', rounded.astype(jnp.float32), value_window.astype(jnp.float32))
    mixed_rows = mixed_rows / jnp.transpose(row_total)[:, :, None]
    return (mixed_rows.astype(jnp.bfloat16), lax.optimization_barrier(jnp.max(row_max, axis=1)))

def orthogonal(matrix):
    highest = lax.Precision.HIGHEST
    identity = jnp.eye(HD, dtype=jnp.float32)
    gram_full = jnp.dot(matrix, matrix.T, preferred_element_type=jnp.float32)
    norm_value = jnp.sqrt(jnp.trace(gram_full)) + norm_eps
    current = matrix.astype(jnp.float32) / norm_value
    for iteration in range(NS_ITERS):
        square = jnp.dot(current, current.T, precision=highest)
        polynomial = first_coef * identity + second_coef * square + third_coef * jnp.dot(square, square, precision=highest)
        current = jnp.dot(polynomial, current, precision=highest)
    return (current * (update_gain * math.sqrt(D))).astype(jnp.bfloat16)

def refresh(triple):
    weight_one, update_one, factor_one = triple
    kept = (1.0 - learn_rate * decay_rate) * weight_one.astype(jnp.float32)
    return (factor_one * (kept - learn_rate * update_one.astype(jnp.float32))).astype(jnp.bfloat16)

def reference(query_vectors, key_vectors, value_vectors, doc_ids, gradients, weights):
    blocks = TOKENS // TOK_DEV
    window = (REACH + 1) * TOK_DEV
    front = REACH * TOK_DEV
    key_padded = jnp.concatenate([jnp.zeros((front, HEADS * HD), key_vectors.dtype), key_vectors], axis=0).reshape(front + TOKENS, HEADS, HD)
    value_padded = jnp.concatenate([jnp.zeros((front, HEADS * HD), value_vectors.dtype), value_vectors], axis=0).reshape(front + TOKENS, HEADS, HD)
    doc_padded = jnp.concatenate([jnp.full((front,), -1, jnp.int32), doc_ids.astype(jnp.int32)], axis=0)
    query_shaped = query_vectors.reshape(blocks, TOK_DEV, HEADS, HD)

    def one_block(block_index):
        begin = (block_index * TOK_DEV).astype(jnp.int32)
        key_window = lax.dynamic_slice_in_dim(key_padded, begin, window, 0)
        value_window = lax.dynamic_slice_in_dim(value_padded, begin, window, 0)
        doc_window = lax.dynamic_slice_in_dim(doc_padded, begin, window, 0)
        doc_block = lax.dynamic_slice_in_dim(doc_ids.astype(jnp.int32), begin, TOK_DEV, 0)
        query_place = front + jnp.arange(TOK_DEV, dtype=jnp.int32)
        key_place = jnp.arange(window, dtype=jnp.int32)
        same_doc = (doc_block[:, None] == doc_window[None, :]) & (key_place[None, :] <= query_place[:, None])
        return block_attention(query_shaped[block_index], key_window, value_window, same_doc)
    mixed_blocks, block_max = lax.map(one_block, jnp.arange(blocks, dtype=jnp.int32))
    attention_out = mixed_blocks.reshape(TOKENS, HEADS * HD)
    max_logit = lax.optimization_barrier(jnp.max(block_max, axis=0))
    root_gamma = jnp.sqrt(clip_tau / jnp.maximum(max_logit, clip_tau))
    update = lax.map(orthogonal, gradients)
    matrix_index = jnp.arange(MATS, dtype=jnp.int32)
    factor = jnp.where(matrix_index < 2 * HEADS, root_gamma[matrix_index % HEADS], 1.0)
    new_weights = lax.map(refresh, (weights, update, factor))
    return (attention_out, update, new_weights)
```

```python
import math

import jax
import jax.numpy as jnp
from jax import lax
from jax.sharding import PartitionSpec as P

D = 7168
HD = 128
REACH = 2
NS_ITERS = 5


first_coef = 3.4445
second_coef = -4.775
third_coef = 2.0315
clip_tau = 100.0
learn_rate = 0.1
decay_rate = 0.1
norm_eps = 1e-07
update_gain = 0.2
masked_fill = -1e30


def shifted(shard, axis, by):
    size = lax.axis_size(axis)
    pairs = [(i, i + by) for i in range(size) if 0 <= i + by < size]
    return lax.ppermute(shard, axis, pairs)


def polynomial_of(square, identity):
    highest = lax.Precision.HIGHEST
    return (
        first_coef * identity
        + second_coef * square
        + third_coef * jnp.matmul(square, square, precision=highest)
    )


def gathered(values, axis):
    size = lax.axis_size(axis)
    spread = jnp.broadcast_to(values[None], (size,) + values.shape)
    return lax.all_to_all(spread, axis, 0, 0, tiled=True)


def shards(query_vectors, key_vectors, value_vectors, doc_ids, gradients, weights):
    highest = lax.Precision.HIGHEST
    tokens_here = query_vectors.shape[0]
    heads_here = query_vectors.shape[1] // HD
    seq_index = lax.axis_index("seq")
    head_index = lax.axis_index("head")
    head_count = lax.axis_size("head")
    local_block = (key_vectors, value_vectors, doc_ids)
    earlier = [shifted(local_block, "seq", distance) for distance in range(1, REACH + 1)]
    ordered = [earlier[REACH - 1 - position] for position in range(REACH)] + [local_block]
    keys_all = jnp.concatenate([member[0] for member in ordered], axis=0)
    values_all = jnp.concatenate([member[1] for member in ordered], axis=0)
    docs_all = jnp.concatenate([member[2] for member in ordered], axis=0)
    key_place = (seq_index - REACH) * tokens_here + jnp.arange(
        (REACH + 1) * tokens_here, dtype=jnp.int32
    )
    query_place = seq_index * tokens_here + jnp.arange(tokens_here, dtype=jnp.int32)
    same_doc = (
        (doc_ids[:, None] == docs_all[None, :])
        & (key_place[None, :] <= query_place[:, None])
        & (key_place[None, :] >= 0)
    )

    def one_head(head_slot):
        col_start = head_slot * HD
        query_cols = lax.dynamic_slice_in_dim(query_vectors, col_start, HD, 1)
        key_cols = lax.dynamic_slice_in_dim(keys_all, col_start, HD, 1)
        value_cols = lax.dynamic_slice_in_dim(values_all, col_start, HD, 1)
        scores = jnp.einsum(
            "qd,kd->qk", query_cols, key_cols, preferred_element_type=jnp.float32
        ) / math.sqrt(HD)
        masked = jnp.where(same_doc, scores, masked_fill)
        row_max = jnp.max(masked, axis=1)
        exp_scores = jnp.exp(masked - row_max[:, None])
        row_total = jnp.sum(exp_scores, axis=1)
        mixed_rows = (
            jnp.dot(exp_scores.astype(jnp.bfloat16), value_cols, preferred_element_type=jnp.float32)
            / row_total[:, None]
        )
        return (mixed_rows.astype(jnp.bfloat16), jnp.max(row_max))

    mixed_heads, head_max = lax.map(one_head, jnp.arange(heads_here, dtype=jnp.int32))
    attention_out = jnp.transpose(mixed_heads, (1, 0, 2)).reshape(tokens_here, heads_here * HD)
    heads_all = heads_here * head_count
    head_slots = jnp.arange(heads_all, dtype=jnp.int32)
    seq_max = jnp.max(gathered(head_max, "seq"), axis=0)
    max_logit = gathered(seq_max, "head").reshape(heads_all)
    root_gamma = jnp.sqrt(clip_tau / jnp.maximum(max_logit, clip_tau))

    pieces = gathered(gradients, "head")
    mats_here, rows_here = gradients.shape[0], gradients.shape[1]
    cols_here = weights.shape[2]
    gram = jnp.einsum(
        "jmrd,kmsd->mjrks", pieces, pieces, preferred_element_type=jnp.float32
    ).reshape(mats_here, HD, HD)
    norm_value = jnp.sqrt(jnp.trace(gram, axis1=1, axis2=2)) + norm_eps
    square = gram / (norm_value * norm_value)[:, None, None]
    identity = jnp.eye(HD, dtype=jnp.float32)
    total = None
    for iteration in range(NS_ITERS):
        poly = polynomial_of(square, identity)
        total = poly if total is None else jnp.matmul(poly, total, precision=highest)
        if iteration + 1 < NS_ITERS:
            square = jnp.matmul(
                poly, jnp.matmul(square, poly, precision=highest), precision=highest
            )
    own_cols = lax.dynamic_slice_in_dim(pieces, head_index * cols_here, cols_here, 3)
    start = own_cols.astype(jnp.float32) / norm_value[None, :, None, None]
    current = jnp.einsum(
        "mijr,jmrd->mid",
        total.reshape(mats_here, HD, head_count, rows_here),
        start,
        precision=highest,
    )
    update = (current * (update_gain * math.sqrt(D))).astype(jnp.bfloat16)
    matrix_index = seq_index * mats_here + jnp.arange(mats_here, dtype=jnp.int32)
    one_hot = (matrix_index[:, None] % heads_all == head_slots[None, :]).astype(jnp.float32)
    picked = jnp.sum(one_hot * root_gamma[None, :], axis=1)
    factor = jnp.where(matrix_index < 2 * heads_all, picked, 1.0)
    kept = (1.0 - learn_rate * decay_rate) * weights.astype(jnp.float32)
    new_weights = (factor[:, None, None] * (kept - learn_rate * update.astype(jnp.float32))).astype(
        jnp.bfloat16
    )
    return (attention_out, update, new_weights)


def solution(mesh):
    return jax.shard_map(
        shards,
        mesh=mesh,
        in_specs=(
            P("seq", "head"),
            P("seq", "head"),
            P("seq", "head"),
            P("seq"),
            P("seq", "head", None),
            P("seq", None, "head"),
        ),
        out_specs=(P("seq", "head"), P("seq", None, "head"), P("seq", None, "head")),
        check_vma=False,
    )
```

```python
import math

import jax
import jax.numpy as jnp
from jax import lax
from jax.sharding import PartitionSpec as P

D = 7168
HD = 128
REACH = 2
NS_ITERS = 5


first_coef = 3.4445
second_coef = -4.775
third_coef = 2.0315
clip_tau = 100.0
learn_rate = 0.1
decay_rate = 0.1
norm_eps = 1e-07
update_gain = 0.2
masked_fill = -1e30


def shifted(shard, axis, by):
    size = lax.axis_size(axis)
    pairs = [(i, i + by) for i in range(size) if 0 <= i + by < size]
    return lax.ppermute(shard, axis, pairs)


def polynomial_of(square, identity):
    highest = lax.Precision.HIGHEST
    return (
        first_coef * identity
        + second_coef * square
        + third_coef * jnp.matmul(square, square, precision=highest)
    )


def gathered(values, axis):
    size = lax.axis_size(axis)
    spread = jnp.broadcast_to(values[None], (size,) + values.shape)
    return lax.all_to_all(spread, axis, 0, 0, tiled=True)


def shards(query_vectors, key_vectors, value_vectors, doc_ids, gradients, weights):
    highest = lax.Precision.HIGHEST
    tokens_here = query_vectors.shape[0]
    heads_here = query_vectors.shape[1] // HD
    seq_index = lax.axis_index("seq")
    head_index = lax.axis_index("head")
    head_count = lax.axis_size("head")
    pieces = gathered(gradients, "head")
    mats_here, rows_here = gradients.shape[0], gradients.shape[1]
    cols_here = weights.shape[2]
    gram = jnp.einsum(
        "jmrd,kmsd->mjrks", pieces, pieces, preferred_element_type=jnp.float32
    ).reshape(mats_here, HD, HD)
    norm_value = jnp.sqrt(jnp.trace(gram, axis1=1, axis2=2)) + norm_eps
    square = gram / (norm_value * norm_value)[:, None, None]
    identity = jnp.eye(HD, dtype=jnp.float32)
    total = None
    for iteration in range(NS_ITERS):
        poly = polynomial_of(square, identity)
        total = poly if total is None else jnp.matmul(poly, total, precision=highest)
        if iteration + 1 < NS_ITERS:
            square = jnp.matmul(
                poly, jnp.matmul(square, poly, precision=highest), precision=highest
            )
    own_cols = lax.dynamic_slice_in_dim(pieces, head_index * cols_here, cols_here, 3)
    start = own_cols.astype(jnp.float32) / norm_value[None, :, None, None]
    current = jnp.einsum(
        "mijr,jmrd->mid",
        total.reshape(mats_here, HD, head_count, rows_here),
        start,
        precision=highest,
    )
    update = (current * (update_gain * math.sqrt(D))).astype(jnp.bfloat16)
    update, query_vectors = lax.optimization_barrier((update, query_vectors))
    local_block = (key_vectors, value_vectors, doc_ids)
    earlier = []
    passed = local_block
    for distance in range(REACH):
        passed = shifted(passed, "seq", 1)
        earlier.append(passed)
    ordered = [earlier[REACH - 1 - position] for position in range(REACH)] + [local_block]
    keys_all = jnp.concatenate([member[0] for member in ordered], axis=0)
    values_all = jnp.concatenate([member[1] for member in ordered], axis=0)
    docs_all = jnp.concatenate([member[2] for member in ordered], axis=0)
    key_place = (seq_index - REACH) * tokens_here + jnp.arange(
        (REACH + 1) * tokens_here, dtype=jnp.int32
    )
    query_place = seq_index * tokens_here + jnp.arange(tokens_here, dtype=jnp.int32)
    same_doc = (
        (doc_ids[:, None] == docs_all[None, :])
        & (key_place[None, :] <= query_place[:, None])
        & (key_place[None, :] >= 0)
    )

    def one_head(head_slot):
        col_start = head_slot * HD
        query_cols = lax.dynamic_slice_in_dim(query_vectors, col_start, HD, 1)
        key_cols = lax.dynamic_slice_in_dim(keys_all, col_start, HD, 1)
        value_cols = lax.dynamic_slice_in_dim(values_all, col_start, HD, 1)
        scores = jnp.einsum(
            "qd,kd->qk", query_cols, key_cols, preferred_element_type=jnp.float32
        ) / math.sqrt(HD)
        masked = jnp.where(same_doc, scores, masked_fill)
        row_max = jnp.max(masked, axis=1)
        exp_scores = jnp.exp(masked - row_max[:, None])
        row_total = jnp.sum(exp_scores, axis=1)
        mixed_rows = (
            jnp.dot(exp_scores.astype(jnp.bfloat16), value_cols, preferred_element_type=jnp.float32)
            / row_total[:, None]
        )
        return (mixed_rows.astype(jnp.bfloat16), jnp.max(row_max))

    mixed_heads, head_max = lax.map(one_head, jnp.arange(heads_here, dtype=jnp.int32))
    attention_out = jnp.transpose(mixed_heads, (1, 0, 2)).reshape(tokens_here, heads_here * HD)
    heads_all = heads_here * head_count
    head_slots = jnp.arange(heads_all, dtype=jnp.int32)
    seq_max = jnp.max(gathered(head_max, "seq"), axis=0)
    max_logit = gathered(seq_max, "head").reshape(heads_all)
    root_gamma = jnp.sqrt(clip_tau / jnp.maximum(max_logit, clip_tau))

    matrix_index = seq_index * mats_here + jnp.arange(mats_here, dtype=jnp.int32)
    one_hot = (matrix_index[:, None] % heads_all == head_slots[None, :]).astype(jnp.float32)
    picked = jnp.sum(one_hot * root_gamma[None, :], axis=1)
    factor = jnp.where(matrix_index < 2 * heads_all, picked, 1.0)
    kept = (1.0 - learn_rate * decay_rate) * weights.astype(jnp.float32)
    new_weights = (factor[:, None, None] * (kept - learn_rate * update.astype(jnp.float32))).astype(
        jnp.bfloat16
    )
    return (attention_out, update, new_weights)


def solution(mesh):
    return jax.shard_map(
        shards,
        mesh=mesh,
        in_specs=(
            P("seq", "head"),
            P("seq", "head"),
            P("seq", "head"),
            P("seq"),
            P("seq", "head", None),
            P("seq", None, "head"),
        ),
        out_specs=(P("seq", "head"), P("seq", None, "head"), P("seq", None, "head")),
        check_vma=False,
    )
```

```python
import math

import jax
import jax.numpy as jnp
from jax import lax
from jax.sharding import PartitionSpec as P

D = 7168
HD = 128
REACH = 2
NS_ITERS = 5


first_coef = 3.4445
second_coef = -4.775
third_coef = 2.0315
clip_tau = 100.0
learn_rate = 0.1
decay_rate = 0.1
norm_eps = 1e-07
update_gain = 0.2
masked_fill = -1e30


def shifted(shard, axis, by):
    size = lax.axis_size(axis)
    pairs = [(i, i + by) for i in range(size) if 0 <= i + by < size]
    return lax.ppermute(shard, axis, pairs)


def polynomial_of(square, identity):
    highest = lax.Precision.HIGHEST
    return (
        first_coef * identity
        + second_coef * square
        + third_coef * jnp.matmul(square, square, precision=highest)
    )


def gathered(values, axis):
    size = lax.axis_size(axis)
    spread = jnp.broadcast_to(values[None], (size,) + values.shape)
    return lax.all_to_all(spread, axis, 0, 0, tiled=True)


def shards(query_vectors, key_vectors, value_vectors, doc_ids, gradients, weights):
    highest = lax.Precision.HIGHEST
    tokens_here = query_vectors.shape[0]
    heads_here = query_vectors.shape[1] // HD
    seq_index = lax.axis_index("seq")
    head_index = lax.axis_index("head")
    head_count = lax.axis_size("head")
    pieces = gathered(gradients, "head")
    mats_here, rows_here = gradients.shape[0], gradients.shape[1]
    cols_here = weights.shape[2]
    gram = jnp.einsum(
        "jmrd,kmsd->mjrks", pieces, pieces, preferred_element_type=jnp.float32
    ).reshape(mats_here, HD, HD)
    norm_value = jnp.sqrt(jnp.trace(gram, axis1=1, axis2=2)) + norm_eps
    square = gram / (norm_value * norm_value)[:, None, None]
    identity = jnp.eye(HD, dtype=jnp.float32)
    total = None
    for iteration in range(NS_ITERS):
        poly = polynomial_of(square, identity)
        total = poly if total is None else jnp.matmul(poly, total, precision=highest)
        if iteration + 1 < NS_ITERS:
            square = jnp.matmul(
                poly, jnp.matmul(square, poly, precision=highest), precision=highest
            )
    own_cols = lax.dynamic_slice_in_dim(pieces, head_index * cols_here, cols_here, 3)
    start = own_cols.astype(jnp.float32) / norm_value[None, :, None, None]
    current = jnp.einsum(
        "mijr,jmrd->mid",
        total.reshape(mats_here, HD, head_count, rows_here),
        start,
        precision=highest,
    )
    update = (current * (update_gain * math.sqrt(D))).astype(jnp.bfloat16)
    local_block = (key_vectors, value_vectors, doc_ids)
    query_place = seq_index * tokens_here + jnp.arange(tokens_here, dtype=jnp.int32)
    def block_max(member, block):
        keys_blk, docs_blk = member[0], member[2]
        place_blk = (seq_index - REACH + block) * tokens_here + jnp.arange(
            tokens_here, dtype=jnp.int32
        )
        allowed = (
            (doc_ids[:, None] == docs_blk[None, :])
            & (place_blk[None, :] <= query_place[:, None])
            & (place_blk[None, :] >= 0)
        )
        found = []
        for head_slot in range(heads_here):
            cols = slice(head_slot * HD, (head_slot + 1) * HD)
            scores = jnp.einsum(
                "qd,kd->qk", query_vectors[:, cols], keys_blk[:, cols],
                preferred_element_type=jnp.float32,
            ) / math.sqrt(HD)
            found.append(jnp.max(jnp.where(allowed, scores, masked_fill)))
        return jnp.stack(found)

    first = shifted(local_block, "seq", 1)
    local_max = block_max(local_block, REACH)
    first, local_max = lax.optimization_barrier((first, local_max))
    second = shifted(first, "seq", 1)
    first_max = block_max(first, REACH - 1)
    second, first_max, update = lax.optimization_barrier((second, first_max, update))
    head_max = jnp.maximum(jnp.maximum(local_max, first_max), block_max(second, REACH - 2))
    earlier = [first, second]
    ordered = [earlier[REACH - 1 - position] for position in range(REACH)] + [local_block]
    keys_all = jnp.concatenate([member[0] for member in ordered], axis=0)
    values_all = jnp.concatenate([member[1] for member in ordered], axis=0)
    docs_all = jnp.concatenate([member[2] for member in ordered], axis=0)
    key_place = (seq_index - REACH) * tokens_here + jnp.arange(
        (REACH + 1) * tokens_here, dtype=jnp.int32
    )
    same_doc = (
        (doc_ids[:, None] == docs_all[None, :])
        & (key_place[None, :] <= query_place[:, None])
        & (key_place[None, :] >= 0)
    )

    def one_head(head_slot):
        col_start = head_slot * HD
        query_cols = lax.dynamic_slice_in_dim(query_vectors, col_start, HD, 1)
        key_cols = lax.dynamic_slice_in_dim(keys_all, col_start, HD, 1)
        value_cols = lax.dynamic_slice_in_dim(values_all, col_start, HD, 1)
        scores = jnp.einsum(
            "qd,kd->qk", query_cols, key_cols, preferred_element_type=jnp.float32
        ) / math.sqrt(HD)
        masked = jnp.where(same_doc, scores, masked_fill)
        row_max = jnp.max(masked, axis=1)
        exp_scores = jnp.exp(masked - row_max[:, None])
        row_total = jnp.sum(exp_scores, axis=1)
        mixed_rows = (
            jnp.dot(exp_scores.astype(jnp.bfloat16), value_cols, preferred_element_type=jnp.float32)
            / row_total[:, None]
        )
        return (mixed_rows.astype(jnp.bfloat16), jnp.max(row_max))

    mixed_heads, _ = lax.map(one_head, jnp.arange(heads_here, dtype=jnp.int32))
    attention_out = jnp.transpose(mixed_heads, (1, 0, 2)).reshape(tokens_here, heads_here * HD)
    heads_all = heads_here * head_count
    head_slots = jnp.arange(heads_all, dtype=jnp.int32)
    seq_max = jnp.max(gathered(head_max, "seq"), axis=0)
    max_logit = gathered(seq_max, "head").reshape(heads_all)
    root_gamma = jnp.sqrt(clip_tau / jnp.maximum(max_logit, clip_tau))

    matrix_index = seq_index * mats_here + jnp.arange(mats_here, dtype=jnp.int32)
    one_hot = (matrix_index[:, None] % heads_all == head_slots[None, :]).astype(jnp.float32)
    picked = jnp.sum(one_hot * root_gamma[None, :], axis=1)
    factor = jnp.where(matrix_index < 2 * heads_all, picked, 1.0)
    kept = (1.0 - learn_rate * decay_rate) * weights.astype(jnp.float32)
    new_weights = (factor[:, None, None] * (kept - learn_rate * update.astype(jnp.float32))).astype(
        jnp.bfloat16
    )
    return (attention_out, update, new_weights)


def solution(mesh):
    return jax.shard_map(
        shards,
        mesh=mesh,
        in_specs=(
            P("seq", "head"),
            P("seq", "head"),
            P("seq", "head"),
            P("seq"),
            P("seq", "head", None),
            P("seq", None, "head"),
        ),
        out_specs=(P("seq", "head"), P("seq", None, "head"), P("seq", None, "head")),
        check_vma=False,
    )
```

```python
import math

import jax
import jax.numpy as jnp
from jax import lax
from jax.sharding import PartitionSpec as P

D = 7168
HD = 128
REACH = 2
NS_ITERS = 5


first_coef = 3.4445
second_coef = -4.775
third_coef = 2.0315
clip_tau = 100.0
learn_rate = 0.1
decay_rate = 0.1
norm_eps = 1e-07
update_gain = 0.2
masked_fill = -1e30


def shifted(shard, axis, by):
    size = lax.axis_size(axis)
    pairs = [(i, i + by) for i in range(size) if 0 <= i + by < size]
    return lax.ppermute(shard, axis, pairs)


def polynomial_of(square, identity):
    highest = lax.Precision.HIGHEST
    return (
        first_coef * identity
        + second_coef * square
        + third_coef * jnp.matmul(square, square, precision=highest)
    )


def gathered(values, axis):
    size = lax.axis_size(axis)
    spread = jnp.broadcast_to(values[None], (size,) + values.shape)
    return lax.all_to_all(spread, axis, 0, 0, tiled=True)


def shards(query_vectors, key_vectors, value_vectors, doc_ids, gradients, weights):
    highest = lax.Precision.HIGHEST
    tokens_here = query_vectors.shape[0]
    heads_here = query_vectors.shape[1] // HD
    seq_index = lax.axis_index("seq")
    head_index = lax.axis_index("head")
    head_count = lax.axis_size("head")
    pieces = gathered(gradients, "head")
    mats_here, rows_here = gradients.shape[0], gradients.shape[1]
    cols_here = weights.shape[2]
    gram = jnp.einsum(
        "jmrd,kmsd->mjrks", pieces, pieces, preferred_element_type=jnp.float32
    ).reshape(mats_here, HD, HD)
    norm_value = jnp.sqrt(jnp.trace(gram, axis1=1, axis2=2)) + norm_eps
    square = gram / (norm_value * norm_value)[:, None, None]
    identity = jnp.eye(HD, dtype=jnp.float32)
    total = None
    for iteration in range(NS_ITERS):
        poly = polynomial_of(square, identity)
        total = poly if total is None else jnp.matmul(poly, total, precision=highest)
        if iteration + 1 < NS_ITERS:
            square = jnp.matmul(
                poly, jnp.matmul(square, poly, precision=highest), precision=highest
            )
    own_cols = lax.dynamic_slice_in_dim(pieces, head_index * cols_here, cols_here, 3)
    start = own_cols.astype(jnp.float32) / norm_value[None, :, None, None]
    current = jnp.einsum(
        "mijr,jmrd->mid",
        total.reshape(mats_here, HD, head_count, rows_here),
        start,
        precision=highest,
    )
    update = (current * (update_gain * math.sqrt(D))).astype(jnp.bfloat16)
    local_block = (key_vectors, value_vectors, doc_ids)
    query_place = seq_index * tokens_here + jnp.arange(tokens_here, dtype=jnp.int32)
    def block_max(member, block):
        keys_blk, docs_blk = member[0], member[2]
        place_blk = (seq_index - REACH + block) * tokens_here + jnp.arange(
            tokens_here, dtype=jnp.int32
        )
        allowed = (
            (doc_ids[:, None] == docs_blk[None, :])
            & (place_blk[None, :] <= query_place[:, None])
            & (place_blk[None, :] >= 0)
        )
        scores = jnp.einsum(
            "qhd,khd->hqk",
            query_vectors.reshape(tokens_here, heads_here, HD),
            keys_blk.reshape(tokens_here, heads_here, HD),
            preferred_element_type=jnp.float32,
        ) / math.sqrt(HD)
        return jnp.max(jnp.where(allowed[None], scores, masked_fill), axis=(1, 2))

    first = shifted(local_block, "seq", 1)
    local_max = block_max(local_block, REACH)
    first, local_max, update = lax.optimization_barrier((first, local_max, update))
    second = shifted(first, "seq", 1)
    first_max = block_max(first, REACH - 1)
    second, first_max = lax.optimization_barrier((second, first_max))
    head_max = jnp.maximum(jnp.maximum(local_max, first_max), block_max(second, REACH - 2))
    earlier = [first, second]
    ordered = [earlier[REACH - 1 - position] for position in range(REACH)] + [local_block]
    keys_all = jnp.concatenate([member[0] for member in ordered], axis=0)
    values_all = jnp.concatenate([member[1] for member in ordered], axis=0)
    docs_all = jnp.concatenate([member[2] for member in ordered], axis=0)
    key_place = (seq_index - REACH) * tokens_here + jnp.arange(
        (REACH + 1) * tokens_here, dtype=jnp.int32
    )
    same_doc = (
        (doc_ids[:, None] == docs_all[None, :])
        & (key_place[None, :] <= query_place[:, None])
        & (key_place[None, :] >= 0)
    )

    def one_head(head_slot):
        col_start = head_slot * HD
        query_cols = lax.dynamic_slice_in_dim(query_vectors, col_start, HD, 1)
        key_cols = lax.dynamic_slice_in_dim(keys_all, col_start, HD, 1)
        value_cols = lax.dynamic_slice_in_dim(values_all, col_start, HD, 1)
        scores = jnp.einsum(
            "qd,kd->qk", query_cols, key_cols, preferred_element_type=jnp.float32
        ) / math.sqrt(HD)
        masked = jnp.where(same_doc, scores, masked_fill)
        row_max = jnp.max(masked, axis=1)
        exp_scores = jnp.exp(masked - row_max[:, None])
        row_total = jnp.sum(exp_scores, axis=1)
        mixed_rows = (
            jnp.dot(exp_scores.astype(jnp.bfloat16), value_cols, preferred_element_type=jnp.float32)
            / row_total[:, None]
        )
        return (mixed_rows.astype(jnp.bfloat16), jnp.max(row_max))

    mixed_heads, _ = lax.map(one_head, jnp.arange(heads_here, dtype=jnp.int32))
    attention_out = jnp.transpose(mixed_heads, (1, 0, 2)).reshape(tokens_here, heads_here * HD)
    heads_all = heads_here * head_count
    head_slots = jnp.arange(heads_all, dtype=jnp.int32)
    seq_max = jnp.max(gathered(head_max, "seq"), axis=0)
    max_logit = gathered(seq_max, "head").reshape(heads_all)
    root_gamma = jnp.sqrt(clip_tau / jnp.maximum(max_logit, clip_tau))

    matrix_index = seq_index * mats_here + jnp.arange(mats_here, dtype=jnp.int32)
    one_hot = (matrix_index[:, None] % heads_all == head_slots[None, :]).astype(jnp.float32)
    picked = jnp.sum(one_hot * root_gamma[None, :], axis=1)
    factor = jnp.where(matrix_index < 2 * heads_all, picked, 1.0)
    kept = (1.0 - learn_rate * decay_rate) * weights.astype(jnp.float32)
    new_weights = (factor[:, None, None] * (kept - learn_rate * update.astype(jnp.float32))).astype(
        jnp.bfloat16
    )
    return (attention_out, update, new_weights)


def solution(mesh):
    return jax.shard_map(
        shards,
        mesh=mesh,
        in_specs=(
            P("seq", "head"),
            P("seq", "head"),
            P("seq", "head"),
            P("seq"),
            P("seq", "head", None),
            P("seq", None, "head"),
        ),
        out_specs=(P("seq", "head"), P("seq", None, "head"), P("seq", None, "head")),
        check_vma=False,
    )
```

```python
import math

import jax
import jax.numpy as jnp
from jax import lax
from jax.sharding import PartitionSpec as P

D = 7168
HD = 128
REACH = 2
NS_ITERS = 5


first_coef = 3.4445
second_coef = -4.775
third_coef = 2.0315
clip_tau = 100.0
learn_rate = 0.1
decay_rate = 0.1
norm_eps = 1e-07
update_gain = 0.2
masked_fill = -1e30


def shifted(shard, axis, by):
    size = lax.axis_size(axis)
    pairs = [(i, i + by) for i in range(size) if 0 <= i + by < size]
    return lax.ppermute(shard, axis, pairs)


def polynomial_of(square, identity):
    highest = lax.Precision.HIGHEST
    return (
        first_coef * identity
        + second_coef * square
        + third_coef * jnp.matmul(square, square, precision=highest)
    )


def gathered(values, axis):
    size = lax.axis_size(axis)
    spread = jnp.broadcast_to(values[None], (size,) + values.shape)
    return lax.all_to_all(spread, axis, 0, 0, tiled=True)


def shards(query_vectors, key_vectors, value_vectors, doc_ids, gradients, weights):
    highest = lax.Precision.HIGHEST
    tokens_here = query_vectors.shape[0]
    heads_here = query_vectors.shape[1] // HD
    seq_index = lax.axis_index("seq")
    head_index = lax.axis_index("head")
    head_count = lax.axis_size("head")
    pieces = gathered(gradients, "head")
    mats_here, rows_here = gradients.shape[0], gradients.shape[1]
    cols_here = weights.shape[2]
    gram = jnp.einsum(
        "jmrd,kmsd->mjrks", pieces, pieces, preferred_element_type=jnp.float32
    ).reshape(mats_here, HD, HD)
    norm_value = jnp.sqrt(jnp.trace(gram, axis1=1, axis2=2)) + norm_eps
    square = gram / (norm_value * norm_value)[:, None, None]
    identity = jnp.eye(HD, dtype=jnp.float32)
    total = None
    for iteration in range(NS_ITERS):
        poly = polynomial_of(square, identity)
        total = poly if total is None else jnp.matmul(poly, total, precision=highest)
        if iteration + 1 < NS_ITERS:
            square = jnp.matmul(
                poly, jnp.matmul(square, poly, precision=highest), precision=highest
            )
    own_cols = lax.dynamic_slice_in_dim(pieces, head_index * cols_here, cols_here, 3)
    start = own_cols.astype(jnp.float32) / norm_value[None, :, None, None]
    current = jnp.einsum(
        "mijr,jmrd->mid",
        total.reshape(mats_here, HD, head_count, rows_here),
        start,
        precision=highest,
    )
    update = (current * (update_gain * math.sqrt(D))).astype(jnp.bfloat16)
    local_block = (key_vectors, value_vectors, doc_ids)
    query_place = seq_index * tokens_here + jnp.arange(tokens_here, dtype=jnp.int32)
    def block_max(member, block):
        keys_blk, docs_blk = member[0], member[2]
        place_blk = (seq_index - REACH + block) * tokens_here + jnp.arange(
            tokens_here, dtype=jnp.int32
        )
        allowed = (
            (doc_ids[:, None] == docs_blk[None, :])
            & (place_blk[None, :] <= query_place[:, None])
            & (place_blk[None, :] >= 0)
        )
        scores = jnp.einsum(
            "qhd,khd->hqk",
            query_vectors.reshape(tokens_here, heads_here, HD),
            keys_blk.reshape(tokens_here, heads_here, HD),
            preferred_element_type=jnp.float32,
        ) / math.sqrt(HD)
        return jnp.max(jnp.where(allowed[None], scores, masked_fill), axis=(1, 2))

    first = shifted(local_block, "seq", 1)
    local_max = block_max(local_block, REACH)
    first, local_max = lax.optimization_barrier((first, local_max))
    second = shifted(first, "seq", 1)
    first_max = block_max(first, REACH - 1)
    second, first_max, update = lax.optimization_barrier((second, first_max, update))
    head_max = jnp.maximum(jnp.maximum(local_max, first_max), block_max(second, REACH - 2))
    earlier = [first, second]
    ordered = [earlier[REACH - 1 - position] for position in range(REACH)] + [local_block]
    keys_all = jnp.concatenate([member[0] for member in ordered], axis=0)
    values_all = jnp.concatenate([member[1] for member in ordered], axis=0)
    docs_all = jnp.concatenate([member[2] for member in ordered], axis=0)
    key_place = (seq_index - REACH) * tokens_here + jnp.arange(
        (REACH + 1) * tokens_here, dtype=jnp.int32
    )
    same_doc = (
        (doc_ids[:, None] == docs_all[None, :])
        & (key_place[None, :] <= query_place[:, None])
        & (key_place[None, :] >= 0)
    )

    def one_head(head_slot):
        col_start = head_slot * HD
        query_cols = lax.dynamic_slice_in_dim(query_vectors, col_start, HD, 1)
        key_cols = lax.dynamic_slice_in_dim(keys_all, col_start, HD, 1)
        value_cols = lax.dynamic_slice_in_dim(values_all, col_start, HD, 1)
        scores = jnp.einsum(
            "qd,kd->qk", query_cols, key_cols, preferred_element_type=jnp.float32
        ) / math.sqrt(HD)
        masked = jnp.where(same_doc, scores, masked_fill)
        row_max = jnp.max(masked, axis=1)
        exp_scores = jnp.exp(masked - row_max[:, None])
        row_total = jnp.sum(exp_scores, axis=1)
        mixed_rows = (
            jnp.dot(exp_scores.astype(jnp.bfloat16), value_cols, preferred_element_type=jnp.float32)
            / row_total[:, None]
        )
        return (mixed_rows.astype(jnp.bfloat16), jnp.max(row_max))

    mixed_heads, _ = lax.map(one_head, jnp.arange(heads_here, dtype=jnp.int32))
    attention_out = jnp.transpose(mixed_heads, (1, 0, 2)).reshape(tokens_here, heads_here * HD)
    heads_all = heads_here * head_count
    head_slots = jnp.arange(heads_all, dtype=jnp.int32)
    seq_max = jnp.max(gathered(head_max, "seq"), axis=0)
    max_logit = gathered(seq_max, "head").reshape(heads_all)
    root_gamma = jnp.sqrt(clip_tau / jnp.maximum(max_logit, clip_tau))

    matrix_index = seq_index * mats_here + jnp.arange(mats_here, dtype=jnp.int32)
    one_hot = (matrix_index[:, None] % heads_all == head_slots[None, :]).astype(jnp.float32)
    picked = jnp.sum(one_hot * root_gamma[None, :], axis=1)
    factor = jnp.where(matrix_index < 2 * heads_all, picked, 1.0)
    kept = (1.0 - learn_rate * decay_rate) * weights.astype(jnp.float32)
    new_weights = (factor[:, None, None] * (kept - learn_rate * update.astype(jnp.float32))).astype(
        jnp.bfloat16
    )
    return (attention_out, update, new_weights)


def solution(mesh):
    return jax.shard_map(
        shards,
        mesh=mesh,
        in_specs=(
            P("seq", "head"),
            P("seq", "head"),
            P("seq", "head"),
            P("seq"),
            P("seq", "head", None),
            P("seq", None, "head"),
        ),
        out_specs=(P("seq", "head"), P("seq", None, "head"), P("seq", None, "head")),
        check_vma=False,
    )
```

```python
import math

import jax
import jax.numpy as jnp
from jax import lax
from jax.sharding import PartitionSpec as P

D = 7168
HD = 128
REACH = 2
NS_ITERS = 5


first_coef = 3.4445
second_coef = -4.775
third_coef = 2.0315
clip_tau = 100.0
learn_rate = 0.1
decay_rate = 0.1
norm_eps = 1e-07
update_gain = 0.2
masked_fill = -1e30


def shifted(shard, axis, by):
    size = lax.axis_size(axis)
    pairs = [(i, i + by) for i in range(size) if 0 <= i + by < size]
    return lax.ppermute(shard, axis, pairs)


def polynomial_of(square, identity):
    highest = lax.Precision.HIGHEST
    return (
        first_coef * identity
        + second_coef * square
        + third_coef * jnp.matmul(square, square, precision=highest)
    )


def packed(arrays, docs):
    digits = jnp.stack([docs // 256, docs % 256], axis=1).astype(jnp.bfloat16)
    tail = jnp.pad(digits, ((0, 0), (0, HD - 2)))
    return jnp.concatenate(list(arrays) + [tail], axis=1)


def unpacked(block, parts, width):
    arrays = [block[:, i * width:(i + 1) * width] for i in range(parts)]
    digits = block[:, parts * width:parts * width + 2].astype(jnp.int32)
    return arrays, digits[:, 0] * 256 + digits[:, 1]


def gathered(values, axis):
    size = lax.axis_size(axis)
    spread = jnp.broadcast_to(values[None], (size,) + values.shape)
    return lax.all_to_all(spread, axis, 0, 0, tiled=True)


def shards(query_vectors, key_vectors, value_vectors, doc_ids, gradients, weights):
    highest = lax.Precision.HIGHEST
    tokens_here = query_vectors.shape[0]
    heads_here = query_vectors.shape[1] // HD
    seq_index = lax.axis_index("seq")
    head_index = lax.axis_index("head")
    head_count = lax.axis_size("head")
    owned = lax.all_to_all(gradients, "head", split_axis=2, concat_axis=1, tiled=True)
    mats_here, rows_here = gradients.shape[0], gradients.shape[1]
    gram_part = jnp.einsum("mid,mjd->mij", owned, owned, preferred_element_type=jnp.float32)
    chunks = jnp.transpose(gram_part.reshape(mats_here, head_count, rows_here, HD), (1, 0, 2, 3))
    rows_mine = jnp.sum(lax.all_to_all(chunks, "head", 0, 0, tiled=True), axis=0)
    gram = jnp.transpose(gathered(rows_mine, "head"), (1, 0, 2, 3)).reshape(mats_here, HD, HD)
    norm_value = jnp.sqrt(jnp.trace(gram, axis1=1, axis2=2)) + norm_eps
    square = gram / (norm_value * norm_value)[:, None, None]
    identity = jnp.eye(HD, dtype=jnp.float32)
    total = None
    for iteration in range(NS_ITERS):
        poly = polynomial_of(square, identity)
        total = poly if total is None else jnp.matmul(poly, total, precision=highest)
        if iteration + 1 < NS_ITERS:
            square = jnp.matmul(
                poly, jnp.matmul(square, poly, precision=highest), precision=highest
            )
    start = owned.astype(jnp.float32) / norm_value[:, None, None]
    current = jnp.matmul(total, start, precision=highest)
    update = (current * (update_gain * math.sqrt(D))).astype(jnp.bfloat16)
    local_block = (key_vectors, value_vectors, doc_ids)
    query_place = seq_index * tokens_here + jnp.arange(tokens_here, dtype=jnp.int32)
    def block_max(queries, query_docs, query_at, member, block):
        keys_blk, docs_blk = member[0], member[2]
        place_blk = (seq_index - REACH + block) * tokens_here + jnp.arange(
            tokens_here, dtype=jnp.int32
        )
        allowed = (
            (query_docs[:, None] == docs_blk[None, :])
            & (place_blk[None, :] <= query_at[:, None])
            & (place_blk[None, :] >= 0)
            & (query_at[:, None] < lax.axis_size("seq") * tokens_here)
        )
        scores = jnp.einsum(
            "qhd,khd->hqk",
            queries.reshape(tokens_here, heads_here, HD),
            keys_blk.reshape(tokens_here, heads_here, HD),
            preferred_element_type=jnp.float32,
        ) / math.sqrt(HD)
        return jnp.max(jnp.where(allowed[None], scores, masked_fill), axis=(1, 2))

    cols = key_vectors.shape[1]
    first_packed = shifted(packed((key_vectors, value_vectors), doc_ids), "seq", 1)
    back = shifted(packed((query_vectors,), doc_ids), "seq", -1)
    local_max = block_max(query_vectors, doc_ids, query_place, local_block, REACH)
    first_packed, local_max = lax.optimization_barrier((first_packed, local_max))
    second_packed = shifted(first_packed, "seq", 1)
    (first_keys, first_values), first_docs = unpacked(first_packed, 2, cols)
    first = (first_keys, first_values, first_docs)
    (next_queries,), next_docs = unpacked(back, 1, cols)
    first_max = block_max(query_vectors, doc_ids, query_place, first, REACH - 1)
    far_max = block_max(next_queries, next_docs, query_place + tokens_here, first, REACH - 1)
    head_max = jnp.maximum(jnp.maximum(local_max, first_max), far_max)
    seq_max = jnp.max(gathered(head_max, "seq"), axis=0)
    second_packed, seq_max = lax.optimization_barrier((second_packed, seq_max))
    (second_keys, second_values), second_docs = unpacked(second_packed, 2, cols)
    second = (second_keys, second_values, second_docs)
    earlier = [first, second]
    ordered = [earlier[REACH - 1 - position] for position in range(REACH)] + [local_block]
    keys_all = jnp.concatenate([member[0] for member in ordered], axis=0)
    values_all = jnp.concatenate([member[1] for member in ordered], axis=0)
    docs_all = jnp.concatenate([member[2] for member in ordered], axis=0)
    key_place = (seq_index - REACH) * tokens_here + jnp.arange(
        (REACH + 1) * tokens_here, dtype=jnp.int32
    )
    same_doc = (
        (doc_ids[:, None] == docs_all[None, :])
        & (key_place[None, :] <= query_place[:, None])
        & (key_place[None, :] >= 0)
    )

    def one_head(head_slot):
        col_start = head_slot * HD
        query_cols = lax.dynamic_slice_in_dim(query_vectors, col_start, HD, 1)
        key_cols = lax.dynamic_slice_in_dim(keys_all, col_start, HD, 1)
        value_cols = lax.dynamic_slice_in_dim(values_all, col_start, HD, 1)
        scores = jnp.einsum(
            "qd,kd->qk", query_cols, key_cols, preferred_element_type=jnp.float32
        ) / math.sqrt(HD)
        masked = jnp.where(same_doc, scores, masked_fill)
        row_max = jnp.max(masked, axis=1)
        exp_scores = jnp.exp(masked - row_max[:, None])
        row_total = jnp.sum(exp_scores, axis=1)
        mixed_rows = (
            jnp.dot(exp_scores.astype(jnp.bfloat16), value_cols, preferred_element_type=jnp.float32)
            / row_total[:, None]
        )
        return (mixed_rows.astype(jnp.bfloat16), jnp.max(row_max))

    mixed_heads, _ = lax.map(one_head, jnp.arange(heads_here, dtype=jnp.int32))
    attention_out = jnp.transpose(mixed_heads, (1, 0, 2)).reshape(tokens_here, heads_here * HD)
    heads_all = heads_here * head_count
    head_slots = jnp.arange(heads_all, dtype=jnp.int32)
    max_logit = gathered(seq_max, "head").reshape(heads_all)
    root_gamma = jnp.sqrt(clip_tau / jnp.maximum(max_logit, clip_tau))

    matrix_index = seq_index * mats_here + jnp.arange(mats_here, dtype=jnp.int32)
    one_hot = (matrix_index[:, None] % heads_all == head_slots[None, :]).astype(jnp.float32)
    picked = jnp.sum(one_hot * root_gamma[None, :], axis=1)
    factor = jnp.where(matrix_index < 2 * heads_all, picked, 1.0)
    kept = (1.0 - learn_rate * decay_rate) * weights.astype(jnp.float32)
    new_weights = (factor[:, None, None] * (kept - learn_rate * update.astype(jnp.float32))).astype(
        jnp.bfloat16
    )
    return (attention_out, update, new_weights)


def solution(mesh):
    return jax.shard_map(
        shards,
        mesh=mesh,
        in_specs=(
            P("seq", "head"),
            P("seq", "head"),
            P("seq", "head"),
            P("seq"),
            P("seq", "head", None),
            P("seq", None, "head"),
        ),
        out_specs=(P("seq", "head"), P("seq", None, "head"), P("seq", None, "head")),
        check_vma=False,
    )
```

```python
import math

import jax
import jax.numpy as jnp
from jax import lax
from jax.sharding import PartitionSpec as P

D = 7168
HD = 128
REACH = 2
NS_ITERS = 5


first_coef = 3.4445
second_coef = -4.775
third_coef = 2.0315
clip_tau = 100.0
learn_rate = 0.1
decay_rate = 0.1
norm_eps = 1e-07
update_gain = 0.2
masked_fill = -1e30


def shifted(shard, axis, by):
    size = lax.axis_size(axis)
    pairs = [(i, i + by) for i in range(size) if 0 <= i + by < size]
    return lax.ppermute(shard, axis, pairs)


def polynomial_of(square, identity):
    highest = lax.Precision.HIGHEST
    return (
        first_coef * identity
        + second_coef * square
        + third_coef * jnp.matmul(square, square, precision=highest)
    )


def gathered(values, axis):
    size = lax.axis_size(axis)
    spread = jnp.broadcast_to(values[None], (size,) + values.shape)
    return lax.all_to_all(spread, axis, 0, 0, tiled=True)


def shards(query_vectors, key_vectors, value_vectors, doc_ids, gradients, weights):
    highest = lax.Precision.HIGHEST
    tokens_here = query_vectors.shape[0]
    heads_here = query_vectors.shape[1] // HD
    seq_index = lax.axis_index("seq")
    head_index = lax.axis_index("head")
    head_count = lax.axis_size("head")
    pieces = gathered(gradients, "head")
    mats_here, rows_here = gradients.shape[0], gradients.shape[1]
    cols_here = weights.shape[2]
    gram = jnp.einsum(
        "jmrd,kmsd->mjrks", pieces, pieces, preferred_element_type=jnp.float32
    ).reshape(mats_here, HD, HD)
    norm_value = jnp.sqrt(jnp.trace(gram, axis1=1, axis2=2)) + norm_eps
    square = gram / (norm_value * norm_value)[:, None, None]
    identity = jnp.eye(HD, dtype=jnp.float32)
    total = None
    for iteration in range(NS_ITERS):
        poly = polynomial_of(square, identity)
        total = poly if total is None else jnp.matmul(poly, total, precision=highest)
        if iteration + 1 < NS_ITERS:
            square = jnp.matmul(
                poly, jnp.matmul(square, poly, precision=highest), precision=highest
            )
    own_cols = lax.dynamic_slice_in_dim(pieces, head_index * cols_here, cols_here, 3)
    start = own_cols.astype(jnp.float32) / norm_value[None, :, None, None]
    current = jnp.einsum(
        "mijr,jmrd->mid",
        total.reshape(mats_here, HD, head_count, rows_here),
        start,
        precision=highest,
    )
    update = (current * (update_gain * math.sqrt(D))).astype(jnp.bfloat16)
    local_block = (key_vectors, value_vectors, doc_ids)
    query_place = seq_index * tokens_here + jnp.arange(tokens_here, dtype=jnp.int32)
    def block_max(member, block):
        keys_blk, docs_blk = member[0], member[2]
        place_blk = (seq_index - REACH + block) * tokens_here + jnp.arange(
            tokens_here, dtype=jnp.int32
        )
        allowed = (
            (doc_ids[:, None] == docs_blk[None, :])
            & (place_blk[None, :] <= query_place[:, None])
            & (place_blk[None, :] >= 0)
        )
        scores = jnp.einsum(
            "qhd,khd->hqk",
            query_vectors.reshape(tokens_here, heads_here, HD),
            keys_blk.reshape(tokens_here, heads_here, HD),
            preferred_element_type=jnp.float32,
        ) / math.sqrt(HD)
        return jnp.max(jnp.where(allowed[None], scores, masked_fill), axis=(1, 2))

    first = shifted(local_block, "seq", 1)
    local_max = block_max(local_block, REACH)
    first, local_max = lax.optimization_barrier((first, local_max))
    second = shifted(first, "seq", 1)
    first_max = block_max(first, REACH - 1)
    second, first_max, update = lax.optimization_barrier((second, first_max, update))
    head_max = jnp.maximum(jnp.maximum(local_max, first_max), block_max(second, REACH - 2))
    earlier = [first, second]
    ordered = [earlier[REACH - 1 - position] for position in range(REACH)] + [local_block]
    keys_all = jnp.concatenate([member[0] for member in ordered], axis=0)
    values_all = jnp.concatenate([member[1] for member in ordered], axis=0)
    docs_all = jnp.concatenate([member[2] for member in ordered], axis=0)
    key_place = (seq_index - REACH) * tokens_here + jnp.arange(
        (REACH + 1) * tokens_here, dtype=jnp.int32
    )
    same_doc = (
        (doc_ids[:, None] == docs_all[None, :])
        & (key_place[None, :] <= query_place[:, None])
        & (key_place[None, :] >= 0)
    )

    def one_head(head_slot):
        col_start = head_slot * HD
        query_cols = lax.dynamic_slice_in_dim(query_vectors, col_start, HD, 1)
        key_cols = lax.dynamic_slice_in_dim(keys_all, col_start, HD, 1)
        value_cols = lax.dynamic_slice_in_dim(values_all, col_start, HD, 1)
        scores = jnp.einsum(
            "qd,kd->qk", query_cols, key_cols, preferred_element_type=jnp.float32
        ) / math.sqrt(HD)
        masked = jnp.where(same_doc, scores, masked_fill)
        row_max = jnp.max(masked, axis=1)
        exp_scores = jnp.exp(masked - row_max[:, None])
        row_total = jnp.sum(exp_scores, axis=1)
        mixed_rows = (
            jnp.dot(exp_scores.astype(jnp.bfloat16), value_cols, preferred_element_type=jnp.float32)
            / row_total[:, None]
        )
        return (mixed_rows.astype(jnp.bfloat16), jnp.max(row_max))

    attention_out = jnp.concatenate([one_head(slot)[0] for slot in range(heads_here)], axis=1)
    heads_all = heads_here * head_count
    head_slots = jnp.arange(heads_all, dtype=jnp.int32)
    seq_max = jnp.max(gathered(head_max, "seq"), axis=0)
    max_logit = gathered(seq_max, "head").reshape(heads_all)
    root_gamma = jnp.sqrt(clip_tau / jnp.maximum(max_logit, clip_tau))

    matrix_index = seq_index * mats_here + jnp.arange(mats_here, dtype=jnp.int32)
    one_hot = (matrix_index[:, None] % heads_all == head_slots[None, :]).astype(jnp.float32)
    picked = jnp.sum(one_hot * root_gamma[None, :], axis=1)
    factor = jnp.where(matrix_index < 2 * heads_all, picked, 1.0)
    kept = (1.0 - learn_rate * decay_rate) * weights.astype(jnp.float32)
    new_weights = (factor[:, None, None] * (kept - learn_rate * update.astype(jnp.float32))).astype(
        jnp.bfloat16
    )
    return (attention_out, update, new_weights)


def solution(mesh):
    return jax.shard_map(
        shards,
        mesh=mesh,
        in_specs=(
            P("seq", "head"),
            P("seq", "head"),
            P("seq", "head"),
            P("seq"),
            P("seq", "head", None),
            P("seq", None, "head"),
        ),
        out_specs=(P("seq", "head"), P("seq", None, "head"), P("seq", None, "head")),
        check_vma=False,
    )
```

```python
import math

import jax
import jax.numpy as jnp
from jax import lax
from jax.sharding import PartitionSpec as P

D = 7168
HD = 128
REACH = 2
NS_ITERS = 5


first_coef = 3.4445
second_coef = -4.775
third_coef = 2.0315
clip_tau = 100.0
learn_rate = 0.1
decay_rate = 0.1
norm_eps = 1e-07
update_gain = 0.2
masked_fill = -1e30


def shifted(shard, axis, by):
    size = lax.axis_size(axis)
    pairs = [(i, i + by) for i in range(size) if 0 <= i + by < size]
    return lax.ppermute(shard, axis, pairs)


def polynomial_of(square, identity):
    highest = lax.Precision.HIGHEST
    return (
        first_coef * identity
        + second_coef * square
        + third_coef * jnp.matmul(square, square, precision=highest)
    )


def gathered(values, axis):
    size = lax.axis_size(axis)
    spread = jnp.broadcast_to(values[None], (size,) + values.shape)
    return lax.all_to_all(spread, axis, 0, 0, tiled=True)


def shards(query_vectors, key_vectors, value_vectors, doc_ids, gradients, weights):
    highest = lax.Precision.HIGHEST
    tokens_here = query_vectors.shape[0]
    heads_here = query_vectors.shape[1] // HD
    seq_index = lax.axis_index("seq")
    head_index = lax.axis_index("head")
    head_count = lax.axis_size("head")
    pieces = gathered(gradients, "head")
    mats_here, rows_here = gradients.shape[0], gradients.shape[1]
    cols_here = weights.shape[2]
    gram = jnp.einsum(
        "jmrd,kmsd->mjrks", pieces, pieces, preferred_element_type=jnp.float32
    ).reshape(mats_here, HD, HD)
    norm_value = jnp.sqrt(jnp.trace(gram, axis1=1, axis2=2)) + norm_eps
    square = gram / (norm_value * norm_value)[:, None, None]
    identity = jnp.eye(HD, dtype=jnp.float32)
    total = None
    for iteration in range(NS_ITERS):
        poly = polynomial_of(square, identity)
        total = poly if total is None else jnp.matmul(poly, total, precision=highest)
        if iteration + 1 < NS_ITERS:
            square = jnp.matmul(
                poly, jnp.matmul(square, poly, precision=highest), precision=highest
            )
    own_cols = lax.dynamic_slice_in_dim(pieces, head_index * cols_here, cols_here, 3)
    start = own_cols.astype(jnp.float32) / norm_value[None, :, None, None]
    current = jnp.einsum(
        "mijr,jmrd->mid",
        total.reshape(mats_here, HD, head_count, rows_here),
        start,
        precision=highest,
    )
    update = (current * (update_gain * math.sqrt(D))).astype(jnp.bfloat16)
    local_block = (key_vectors, value_vectors, doc_ids)
    query_place = seq_index * tokens_here + jnp.arange(tokens_here, dtype=jnp.int32)
    def block_max(member, block):
        keys_blk, docs_blk = member[0], member[2]
        place_blk = (seq_index - REACH + block) * tokens_here + jnp.arange(
            tokens_here, dtype=jnp.int32
        )
        allowed = (
            (doc_ids[:, None] == docs_blk[None, :])
            & (place_blk[None, :] <= query_place[:, None])
            & (place_blk[None, :] >= 0)
        )
        scores = jnp.einsum(
            "qhd,khd->hqk",
            query_vectors.reshape(tokens_here, heads_here, HD),
            keys_blk.reshape(tokens_here, heads_here, HD),
            preferred_element_type=jnp.float32,
        ) / math.sqrt(HD)
        return jnp.max(jnp.where(allowed[None], scores, masked_fill), axis=(1, 2))

    first = shifted(local_block, "seq", 1)
    local_max = block_max(local_block, REACH)
    first, local_max = lax.optimization_barrier((first, local_max))
    second = shifted(first, "seq", 1)
    first_max = block_max(first, REACH - 1)
    second, first_max, update = lax.optimization_barrier((second, first_max, update))
    head_max = jnp.maximum(jnp.maximum(local_max, first_max), block_max(second, REACH - 2))
    earlier = [first, second]
    ordered = [earlier[REACH - 1 - position] for position in range(REACH)] + [local_block]
    keys_all = jnp.concatenate([member[0] for member in ordered], axis=0)
    values_all = jnp.concatenate([member[1] for member in ordered], axis=0)
    docs_all = jnp.concatenate([member[2] for member in ordered], axis=0)
    key_place = (seq_index - REACH) * tokens_here + jnp.arange(
        (REACH + 1) * tokens_here, dtype=jnp.int32
    )
    same_doc = (
        (doc_ids[:, None] == docs_all[None, :])
        & (key_place[None, :] <= query_place[:, None])
        & (key_place[None, :] >= 0)
    )

    group = 2 if heads_here % 2 == 0 else 1

    def head_group(group_index):
        col_start = group_index * (group * HD)
        query_cols = lax.dynamic_slice_in_dim(query_vectors, col_start, group * HD, 1)
        key_cols = lax.dynamic_slice_in_dim(keys_all, col_start, group * HD, 1)
        value_cols = lax.dynamic_slice_in_dim(values_all, col_start, group * HD, 1)
        scores = jnp.einsum(
            "qhd,khd->hqk",
            query_cols.reshape(tokens_here, group, HD),
            key_cols.reshape(-1, group, HD),
            preferred_element_type=jnp.float32,
        ) / math.sqrt(HD)
        masked = jnp.where(same_doc[None], scores, masked_fill)
        row_max = jnp.max(masked, axis=2)
        exp_scores = jnp.exp(masked - row_max[:, :, None])
        row_total = jnp.sum(exp_scores, axis=2)
        mixed_rows = jnp.einsum(
            "hqk,khd->qhd",
            exp_scores.astype(jnp.bfloat16),
            value_cols.reshape(-1, group, HD),
            preferred_element_type=jnp.float32,
        ) / jnp.transpose(row_total)[:, :, None]
        return mixed_rows.astype(jnp.bfloat16).reshape(tokens_here, group * HD)

    mixed_groups = lax.map(head_group, jnp.arange(heads_here // group, dtype=jnp.int32))
    attention_out = jnp.transpose(mixed_groups, (1, 0, 2)).reshape(tokens_here, heads_here * HD)
    heads_all = heads_here * head_count
    head_slots = jnp.arange(heads_all, dtype=jnp.int32)
    seq_max = jnp.max(gathered(head_max, "seq"), axis=0)
    max_logit = gathered(seq_max, "head").reshape(heads_all)
    root_gamma = jnp.sqrt(clip_tau / jnp.maximum(max_logit, clip_tau))

    matrix_index = seq_index * mats_here + jnp.arange(mats_here, dtype=jnp.int32)
    one_hot = (matrix_index[:, None] % heads_all == head_slots[None, :]).astype(jnp.float32)
    picked = jnp.sum(one_hot * root_gamma[None, :], axis=1)
    factor = jnp.where(matrix_index < 2 * heads_all, picked, 1.0)
    kept = (1.0 - learn_rate * decay_rate) * weights.astype(jnp.float32)
    new_weights = (factor[:, None, None] * (kept - learn_rate * update.astype(jnp.float32))).astype(
        jnp.bfloat16
    )
    return (attention_out, update, new_weights)


def solution(mesh):
    return jax.shard_map(
        shards,
        mesh=mesh,
        in_specs=(
            P("seq", "head"),
            P("seq", "head"),
            P("seq", "head"),
            P("seq"),
            P("seq", "head", None),
            P("seq", None, "head"),
        ),
        out_specs=(P("seq", "head"), P("seq", None, "head"), P("seq", None, "head")),
        check_vma=False,
    )
```

```python
import math

import jax
import jax.numpy as jnp
from jax import lax
from jax.sharding import PartitionSpec as P

D = 7168
HD = 128
REACH = 2
NS_ITERS = 5


first_coef = 3.4445
second_coef = -4.775
third_coef = 2.0315
clip_tau = 100.0
learn_rate = 0.1
decay_rate = 0.1
norm_eps = 1e-07
update_gain = 0.2
masked_fill = -1e30


def shifted(shard, axis, by):
    size = lax.axis_size(axis)
    pairs = [(i, i + by) for i in range(size) if 0 <= i + by < size]
    return lax.ppermute(shard, axis, pairs)


def polynomial_of(square, identity):
    highest = lax.Precision.HIGHEST
    return (
        first_coef * identity
        + second_coef * square
        + third_coef * jnp.matmul(square, square, precision=highest)
    )


def gathered(values, axis):
    size = lax.axis_size(axis)
    spread = jnp.broadcast_to(values[None], (size,) + values.shape)
    return lax.all_to_all(spread, axis, 0, 0, tiled=True)


def shards(query_vectors, key_vectors, value_vectors, doc_ids, gradients, weights):
    highest = lax.Precision.HIGHEST
    tokens_here = query_vectors.shape[0]
    heads_here = query_vectors.shape[1] // HD
    seq_index = lax.axis_index("seq")
    head_index = lax.axis_index("head")
    head_count = lax.axis_size("head")
    pieces = gathered(gradients, "head")
    mats_here, rows_here = gradients.shape[0], gradients.shape[1]
    cols_here = weights.shape[2]
    gram = jnp.einsum(
        "jmrd,kmsd->mjrks", pieces, pieces, preferred_element_type=jnp.float32
    ).reshape(mats_here, HD, HD)
    norm_value = jnp.sqrt(jnp.trace(gram, axis1=1, axis2=2)) + norm_eps
    square = gram / (norm_value * norm_value)[:, None, None]
    identity = jnp.eye(HD, dtype=jnp.float32)
    total = None
    for iteration in range(NS_ITERS):
        poly = polynomial_of(square, identity)
        total = poly if total is None else jnp.matmul(poly, total, precision=highest)
        if iteration + 1 < NS_ITERS:
            square = jnp.matmul(
                poly, jnp.matmul(square, poly, precision=highest), precision=highest
            )
    own_cols = lax.dynamic_slice_in_dim(pieces, head_index * cols_here, cols_here, 3)
    start = own_cols.astype(jnp.float32) / norm_value[None, :, None, None]
    current = jnp.einsum(
        "mijr,jmrd->mid",
        total.reshape(mats_here, HD, head_count, rows_here),
        start,
        precision=highest,
    )
    update = (current * (update_gain * math.sqrt(D))).astype(jnp.bfloat16)
    local_block = (key_vectors, value_vectors, doc_ids)
    query_place = seq_index * tokens_here + jnp.arange(tokens_here, dtype=jnp.int32)
    def block_max(member, block):
        keys_blk, docs_blk = member[0], member[2]
        place_blk = (seq_index - REACH + block) * tokens_here + jnp.arange(
            tokens_here, dtype=jnp.int32
        )
        allowed = (
            (doc_ids[:, None] == docs_blk[None, :])
            & (place_blk[None, :] <= query_place[:, None])
            & (place_blk[None, :] >= 0)
        )
        scores = jnp.einsum(
            "qhd,khd->hqk",
            query_vectors.reshape(tokens_here, heads_here, HD),
            keys_blk.reshape(tokens_here, heads_here, HD),
            preferred_element_type=jnp.float32,
        ) / math.sqrt(HD)
        return jnp.max(jnp.where(allowed[None], scores, masked_fill), axis=(1, 2))

    first = shifted(local_block, "seq", 1)
    local_max = block_max(local_block, REACH)
    first, local_max = lax.optimization_barrier((first, local_max))
    second = shifted(first, "seq", 1)
    first_max = block_max(first, REACH - 1)
    second, first_max, update = lax.optimization_barrier((second, first_max, update))
    head_max = jnp.maximum(jnp.maximum(local_max, first_max), block_max(second, REACH - 2))
    earlier = [first, second]
    ordered = [earlier[REACH - 1 - position] for position in range(REACH)] + [local_block]
    keys_all = jnp.concatenate([member[0] for member in ordered], axis=0)
    values_all = jnp.concatenate([member[1] for member in ordered], axis=0)
    docs_all = jnp.concatenate([member[2] for member in ordered], axis=0)
    key_place = (seq_index - REACH) * tokens_here + jnp.arange(
        (REACH + 1) * tokens_here, dtype=jnp.int32
    )
    same_doc = (
        (doc_ids[:, None] == docs_all[None, :])
        & (key_place[None, :] <= query_place[:, None])
        & (key_place[None, :] >= 0)
    )

    group = 3 if heads_here % 3 == 0 else 1

    def head_group(group_index):
        col_start = group_index * (group * HD)
        query_cols = lax.dynamic_slice_in_dim(query_vectors, col_start, group * HD, 1)
        key_cols = lax.dynamic_slice_in_dim(keys_all, col_start, group * HD, 1)
        value_cols = lax.dynamic_slice_in_dim(values_all, col_start, group * HD, 1)
        scores = jnp.einsum(
            "qhd,khd->hqk",
            query_cols.reshape(tokens_here, group, HD),
            key_cols.reshape(-1, group, HD),
            preferred_element_type=jnp.float32,
        ) / math.sqrt(HD)
        masked = jnp.where(same_doc[None], scores, masked_fill)
        row_max = jnp.max(masked, axis=2)
        exp_scores = jnp.exp(masked - row_max[:, :, None])
        row_total = jnp.sum(exp_scores, axis=2)
        mixed_rows = jnp.einsum(
            "hqk,khd->qhd",
            exp_scores.astype(jnp.bfloat16),
            value_cols.reshape(-1, group, HD),
            preferred_element_type=jnp.float32,
        ) / jnp.transpose(row_total)[:, :, None]
        return mixed_rows.astype(jnp.bfloat16).reshape(tokens_here, group * HD)

    mixed_groups = lax.map(head_group, jnp.arange(heads_here // group, dtype=jnp.int32))
    attention_out = jnp.transpose(mixed_groups, (1, 0, 2)).reshape(tokens_here, heads_here * HD)
    heads_all = heads_here * head_count
    head_slots = jnp.arange(heads_all, dtype=jnp.int32)
    seq_max = jnp.max(gathered(head_max, "seq"), axis=0)
    max_logit = gathered(seq_max, "head").reshape(heads_all)
    root_gamma = jnp.sqrt(clip_tau / jnp.maximum(max_logit, clip_tau))

    matrix_index = seq_index * mats_here + jnp.arange(mats_here, dtype=jnp.int32)
    one_hot = (matrix_index[:, None] % heads_all == head_slots[None, :]).astype(jnp.float32)
    picked = jnp.sum(one_hot * root_gamma[None, :], axis=1)
    factor = jnp.where(matrix_index < 2 * heads_all, picked, 1.0)
    kept = (1.0 - learn_rate * decay_rate) * weights.astype(jnp.float32)
    new_weights = (factor[:, None, None] * (kept - learn_rate * update.astype(jnp.float32))).astype(
        jnp.bfloat16
    )
    return (attention_out, update, new_weights)


def solution(mesh):
    return jax.shard_map(
        shards,
        mesh=mesh,
        in_specs=(
            P("seq", "head"),
            P("seq", "head"),
            P("seq", "head"),
            P("seq"),
            P("seq", "head", None),
            P("seq", None, "head"),
        ),
        out_specs=(P("seq", "head"), P("seq", None, "head"), P("seq", None, "head")),
        check_vma=False,
    )
```

```python
import math

import jax
import jax.numpy as jnp
from jax import lax
from jax.sharding import PartitionSpec as P

D = 7168
HD = 128
REACH = 2
NS_ITERS = 5


first_coef = 3.4445
second_coef = -4.775
third_coef = 2.0315
clip_tau = 100.0
learn_rate = 0.1
decay_rate = 0.1
norm_eps = 1e-07
update_gain = 0.2
masked_fill = -1e30


def shifted(shard, axis, by):
    size = lax.axis_size(axis)
    pairs = [(i, i + by) for i in range(size) if 0 <= i + by < size]
    return lax.ppermute(shard, axis, pairs)


def polynomial_of(square, identity):
    highest = lax.Precision.HIGHEST
    return (
        first_coef * identity
        + second_coef * square
        + third_coef * jnp.matmul(square, square, precision=highest)
    )


def gathered(values, axis):
    size = lax.axis_size(axis)
    spread = jnp.broadcast_to(values[None], (size,) + values.shape)
    return lax.all_to_all(spread, axis, 0, 0, tiled=True)


def shards(query_vectors, key_vectors, value_vectors, doc_ids, gradients, weights):
    highest = lax.Precision.HIGHEST
    tokens_here = query_vectors.shape[0]
    heads_here = query_vectors.shape[1] // HD
    seq_index = lax.axis_index("seq")
    head_index = lax.axis_index("head")
    head_count = lax.axis_size("head")
    pieces = gathered(gradients, "head")
    mats_here, rows_here = gradients.shape[0], gradients.shape[1]
    cols_here = weights.shape[2]
    gram = jnp.einsum(
        "jmrd,kmsd->mjrks", pieces, pieces, preferred_element_type=jnp.float32
    ).reshape(mats_here, HD, HD)
    norm_value = jnp.sqrt(jnp.trace(gram, axis1=1, axis2=2)) + norm_eps
    square = gram / (norm_value * norm_value)[:, None, None]
    identity = jnp.eye(HD, dtype=jnp.float32)
    total = None
    for iteration in range(NS_ITERS):
        poly = polynomial_of(square, identity)
        total = poly if total is None else jnp.matmul(poly, total, precision=highest)
        if iteration + 1 < NS_ITERS:
            square = jnp.matmul(
                poly, jnp.matmul(square, poly, precision=highest), precision=highest
            )
    own_cols = lax.dynamic_slice_in_dim(pieces, head_index * cols_here, cols_here, 3)
    start = own_cols.astype(jnp.float32) / norm_value[None, :, None, None]
    current = jnp.einsum(
        "mijr,jmrd->mid",
        total.reshape(mats_here, HD, head_count, rows_here),
        start,
        precision=highest,
    )
    update = (current * (update_gain * math.sqrt(D))).astype(jnp.bfloat16)
    local_block = (key_vectors, value_vectors, doc_ids)
    query_place = seq_index * tokens_here + jnp.arange(tokens_here, dtype=jnp.int32)
    def block_max(member, block):
        keys_blk, docs_blk = member[0], member[2]
        place_blk = (seq_index - REACH + block) * tokens_here + jnp.arange(
            tokens_here, dtype=jnp.int32
        )
        allowed = (
            (doc_ids[:, None] == docs_blk[None, :])
            & (place_blk[None, :] <= query_place[:, None])
            & (place_blk[None, :] >= 0)
        )
        scores = jnp.einsum(
            "qhd,khd->hqk",
            query_vectors.reshape(tokens_here, heads_here, HD),
            keys_blk.reshape(tokens_here, heads_here, HD),
            preferred_element_type=jnp.float32,
        ) / math.sqrt(HD)
        return jnp.max(jnp.where(allowed[None], scores, masked_fill), axis=(1, 2))

    first = shifted(local_block, "seq", 1)
    local_max = block_max(local_block, REACH)
    first, local_max = lax.optimization_barrier((first, local_max))
    second = shifted(first, "seq", 1)
    first_max = block_max(first, REACH - 1)
    key_window = jnp.concatenate([jnp.zeros_like(key_vectors), first[0], key_vectors], axis=0)
    value_window = jnp.concatenate([jnp.zeros_like(value_vectors), first[1], value_vectors], axis=0)
    second, first_max, update, key_window, value_window = lax.optimization_barrier(
        (second, first_max, update, key_window, value_window)
    )
    head_max = jnp.maximum(jnp.maximum(local_max, first_max), block_max(second, REACH - 2))
    earlier = [first, second]
    ordered = [earlier[REACH - 1 - position] for position in range(REACH)] + [local_block]
    keys_all = lax.dynamic_update_slice_in_dim(key_window, second[0], 0, 0)
    values_all = lax.dynamic_update_slice_in_dim(value_window, second[1], 0, 0)
    docs_all = jnp.concatenate([member[2] for member in ordered], axis=0)
    key_place = (seq_index - REACH) * tokens_here + jnp.arange(
        (REACH + 1) * tokens_here, dtype=jnp.int32
    )
    same_doc = (
        (doc_ids[:, None] == docs_all[None, :])
        & (key_place[None, :] <= query_place[:, None])
        & (key_place[None, :] >= 0)
    )

    group = 2 if heads_here % 2 == 0 else 1

    def head_group(group_index):
        col_start = group_index * (group * HD)
        query_cols = lax.dynamic_slice_in_dim(query_vectors, col_start, group * HD, 1)
        key_cols = lax.dynamic_slice_in_dim(keys_all, col_start, group * HD, 1)
        value_cols = lax.dynamic_slice_in_dim(values_all, col_start, group * HD, 1)
        scores = jnp.einsum(
            "qhd,khd->hqk",
            query_cols.reshape(tokens_here, group, HD),
            key_cols.reshape(-1, group, HD),
            preferred_element_type=jnp.float32,
        ) / math.sqrt(HD)
        masked = jnp.where(same_doc[None], scores, masked_fill)
        row_max = jnp.max(masked, axis=2)
        exp_scores = jnp.exp(masked - row_max[:, :, None])
        row_total = jnp.sum(exp_scores, axis=2)
        mixed_rows = jnp.einsum(
            "hqk,khd->qhd",
            exp_scores.astype(jnp.bfloat16),
            value_cols.reshape(-1, group, HD),
            preferred_element_type=jnp.float32,
        ) / jnp.transpose(row_total)[:, :, None]
        return mixed_rows.astype(jnp.bfloat16).reshape(tokens_here, group * HD)

    mixed_groups = lax.map(head_group, jnp.arange(heads_here // group, dtype=jnp.int32))
    attention_out = jnp.transpose(mixed_groups, (1, 0, 2)).reshape(tokens_here, heads_here * HD)
    heads_all = heads_here * head_count
    head_slots = jnp.arange(heads_all, dtype=jnp.int32)
    seq_max = jnp.max(gathered(head_max, "seq"), axis=0)
    max_logit = gathered(seq_max, "head").reshape(heads_all)
    root_gamma = jnp.sqrt(clip_tau / jnp.maximum(max_logit, clip_tau))

    matrix_index = seq_index * mats_here + jnp.arange(mats_here, dtype=jnp.int32)
    one_hot = (matrix_index[:, None] % heads_all == head_slots[None, :]).astype(jnp.float32)
    picked = jnp.sum(one_hot * root_gamma[None, :], axis=1)
    factor = jnp.where(matrix_index < 2 * heads_all, picked, 1.0)
    kept = (1.0 - learn_rate * decay_rate) * weights.astype(jnp.float32)
    new_weights = (factor[:, None, None] * (kept - learn_rate * update.astype(jnp.float32))).astype(
        jnp.bfloat16
    )
    return (attention_out, update, new_weights)


def solution(mesh):
    return jax.shard_map(
        shards,
        mesh=mesh,
        in_specs=(
            P("seq", "head"),
            P("seq", "head"),
            P("seq", "head"),
            P("seq"),
            P("seq", "head", None),
            P("seq", None, "head"),
        ),
        out_specs=(P("seq", "head"), P("seq", None, "head"), P("seq", None, "head")),
        check_vma=False,
    )
```

```python
import math

import jax
import jax.numpy as jnp
from jax import lax
from jax.sharding import PartitionSpec as P

D = 7168
HD = 128
REACH = 2
NS_ITERS = 5


first_coef = 3.4445
second_coef = -4.775
third_coef = 2.0315
clip_tau = 100.0
learn_rate = 0.1
decay_rate = 0.1
norm_eps = 1e-07
update_gain = 0.2
masked_fill = -1e30


def shifted(shard, axis, by):
    size = lax.axis_size(axis)
    pairs = [(i, i + by) for i in range(size) if 0 <= i + by < size]
    return lax.ppermute(shard, axis, pairs)


def polynomial_of(square, identity):
    highest = lax.Precision.HIGHEST
    return (
        first_coef * identity
        + second_coef * square
        + third_coef * jnp.matmul(square, square, precision=highest)
    )


def gathered(values, axis):
    size = lax.axis_size(axis)
    spread = jnp.broadcast_to(values[None], (size,) + values.shape)
    return lax.all_to_all(spread, axis, 0, 0, tiled=True)


def shards(query_vectors, key_vectors, value_vectors, doc_ids, gradients, weights):
    highest = lax.Precision.HIGHEST
    tokens_here = query_vectors.shape[0]
    heads_here = query_vectors.shape[1] // HD
    seq_index = lax.axis_index("seq")
    head_index = lax.axis_index("head")
    head_count = lax.axis_size("head")
    pieces = gathered(gradients, "head")
    mats_here, rows_here = gradients.shape[0], gradients.shape[1]
    cols_here = weights.shape[2]
    gram = jnp.einsum(
        "jmrd,kmsd->mjrks", pieces, pieces, preferred_element_type=jnp.float32
    ).reshape(mats_here, HD, HD)
    norm_value = jnp.sqrt(jnp.trace(gram, axis1=1, axis2=2)) + norm_eps
    square = gram / (norm_value * norm_value)[:, None, None]
    identity = jnp.eye(HD, dtype=jnp.float32)
    total = None
    for iteration in range(NS_ITERS):
        poly = polynomial_of(square, identity)
        total = poly if total is None else jnp.matmul(poly, total, precision=highest)
        if iteration + 1 < NS_ITERS:
            square = jnp.matmul(
                poly, jnp.matmul(square, poly, precision=highest), precision=highest
            )
    own_cols = lax.dynamic_slice_in_dim(pieces, head_index * cols_here, cols_here, 3)
    start = own_cols.astype(jnp.float32) / norm_value[None, :, None, None]
    current = jnp.einsum(
        "mijr,jmrd->mid",
        total.reshape(mats_here, HD, head_count, rows_here),
        start,
        precision=highest,
    )
    update = (current * (update_gain * math.sqrt(D))).astype(jnp.bfloat16)
    local_block = (key_vectors, value_vectors, doc_ids)
    query_place = seq_index * tokens_here + jnp.arange(tokens_here, dtype=jnp.int32)
    def block_max(member, block):
        keys_blk, docs_blk = member[0], member[2]
        place_blk = (seq_index - REACH + block) * tokens_here + jnp.arange(
            tokens_here, dtype=jnp.int32
        )
        allowed = (
            (doc_ids[:, None] == docs_blk[None, :])
            & (place_blk[None, :] <= query_place[:, None])
            & (place_blk[None, :] >= 0)
        )
        scores = jnp.einsum(
            "qhd,khd->hqk",
            query_vectors.reshape(tokens_here, heads_here, HD),
            keys_blk.reshape(tokens_here, heads_here, HD),
            preferred_element_type=jnp.float32,
        ) / math.sqrt(HD)
        return jnp.max(jnp.where(allowed[None], scores, masked_fill), axis=(1, 2))

    first = shifted(local_block, "seq", 1)
    local_max = block_max(local_block, REACH)
    first, local_max = lax.optimization_barrier((first, local_max))
    second = shifted(first, "seq", 1)
    first_max = block_max(first, REACH - 1)
    second, first_max, update = lax.optimization_barrier((second, first_max, update))
    head_max = jnp.maximum(jnp.maximum(local_max, first_max), block_max(second, REACH - 2))
    earlier = [first, second]
    ordered = [earlier[REACH - 1 - position] for position in range(REACH)] + [local_block]
    keys_all = jnp.concatenate([member[0] for member in ordered], axis=0)
    values_all = jnp.concatenate([member[1] for member in ordered], axis=0)
    docs_all = jnp.concatenate([member[2] for member in ordered], axis=0)
    key_place = (seq_index - REACH) * tokens_here + jnp.arange(
        (REACH + 1) * tokens_here, dtype=jnp.int32
    )
    same_doc = (
        (doc_ids[:, None] == docs_all[None, :])
        & (key_place[None, :] <= query_place[:, None])
        & (key_place[None, :] >= 0)
    )

    group = 2 if heads_here % 2 == 0 else 1

    def head_group(group_index):
        col_start = group_index * (group * HD)
        query_cols = lax.dynamic_slice_in_dim(query_vectors, col_start, group * HD, 1)
        key_cols = lax.dynamic_slice_in_dim(keys_all, col_start, group * HD, 1)
        value_cols = lax.dynamic_slice_in_dim(values_all, col_start, group * HD, 1)
        scores = jnp.einsum(
            "qhd,khd->hqk",
            query_cols.reshape(tokens_here, group, HD),
            key_cols.reshape(-1, group, HD),
            preferred_element_type=jnp.float32,
        ) / math.sqrt(HD)
        masked = jnp.where(same_doc[None], scores, masked_fill)
        row_max = jnp.max(masked, axis=2)
        exp_scores = jnp.exp(masked - row_max[:, :, None])
        row_total = jnp.sum(exp_scores, axis=2)
        mixed_rows = jnp.einsum(
            "hqk,khd->qhd",
            exp_scores.astype(jnp.bfloat16),
            value_cols.reshape(-1, group, HD),
            preferred_element_type=jnp.float32,
        ) / jnp.transpose(row_total)[:, :, None]
        return mixed_rows.astype(jnp.bfloat16).reshape(tokens_here, group * HD)

    mixed_groups = lax.map(head_group, jnp.arange(heads_here // group, dtype=jnp.int32))
    attention_out = jnp.transpose(mixed_groups, (1, 0, 2)).reshape(tokens_here, heads_here * HD)
    heads_all = heads_here * head_count
    head_slots = jnp.arange(heads_all, dtype=jnp.int32)
    block_logit = gathered(head_max, "head").reshape(heads_all)
    seq_count = lax.axis_size("seq")
    wanted = (
        jnp.arange(seq_count, dtype=jnp.int32)[:, None] * mats_here
        + jnp.arange(mats_here, dtype=jnp.int32)[None, :]
    ) % heads_all
    max_logit = jnp.max(lax.all_to_all(block_logit[wanted], "seq", 0, 0, tiled=True), axis=0)
    picked = jnp.sqrt(clip_tau / jnp.maximum(max_logit, clip_tau))

    matrix_index = seq_index * mats_here + jnp.arange(mats_here, dtype=jnp.int32)
    factor = jnp.where(matrix_index < 2 * heads_all, picked, 1.0)
    kept = (1.0 - learn_rate * decay_rate) * weights.astype(jnp.float32)
    new_weights = (factor[:, None, None] * (kept - learn_rate * update.astype(jnp.float32))).astype(
        jnp.bfloat16
    )
    return (attention_out, update, new_weights)


def solution(mesh):
    return jax.shard_map(
        shards,
        mesh=mesh,
        in_specs=(
            P("seq", "head"),
            P("seq", "head"),
            P("seq", "head"),
            P("seq"),
            P("seq", "head", None),
            P("seq", None, "head"),
        ),
        out_specs=(P("seq", "head"), P("seq", None, "head"), P("seq", None, "head")),
        check_vma=False,
    )
```
